128 devices in a mesh: obs: 8 (over z, core), tile: 16 (over x, y).
Axes of the slice: x: 4, y: 4, z: 4, core: 2. Of those that a mesh axis runs over, the one named last changes fastest.
Arguments:
- raw_obs: bfloat16 [4096, 128, 128], P(('obs', 'tile')), may hold values from -6 to 6
- obs_bias: bfloat16 [4096, 128], P(('obs', 'tile')), may hold values from -2 to 302
- instrument: int32 [4096], P(('obs', 'tile')), may hold values from 0 to 5
- owner: int32 [4096, 1], P(('obs', 'tile')), may hold values from 0 to 15; in each aligned block of 32 rows (0 to 31, 32 to 63, ...) at most 4 rows name the same one
- local_tile: int32 [4096], P(('obs', 'tile')), may hold values from 0 to 3
- latents: bfloat16 [8192, 512], P('tile'), may hold values from -6 to 6
- first_weight: bfloat16 [6, 128, 512], replicated, may hold values from -0.5 to 0.5
- second_weight: bfloat16 [6, 512, 512], replicated, may hold values from -0.25 to 0.25
- query_weight: bfloat16 [512, 512], replicated, may hold values from -0.25 to 0.25
- pair_weight: bfloat16 [512, 1024], replicated, may hold values from -0.25 to 0.25
- self_bias: float32 [8], replicated, may hold values from 6 to 9
- out_weight: bfloat16 [512, 512], P(None, 'obs'), may hold values from -0.25 to 0.25
- edge_gain: float32 [512], P('obs'), may hold values from 0.1 to 0.4
Outputs:
- joined_latents: float32 [8192, 512], P('tile', 'obs')
The draws below stay inside these ranges and needn't reach their ends.
Inputs may be any that keep to these rules, and one draw needn't show every extreme that they name: Among the 32 blocks of one device, at most 4 have the same owner, and in every draw some device has exactly 4 blocks for one owner.
All inputs are finite; a program needn't handle non-finite values.
Results may differ from the reference program's by a relative error of at most 0.0036.
Values may be sent and summed in bfloat16 or wider, within the bound.
No kernel may reach another device: no remote copies, remote signals or barrier semaphores. Data moves between devices by JAX's collectives and lax.ppermute only.
A program may use at most 128 MiB of HBM per device.

```python
import math
import jax
import jax.numpy as jnp
import numpy as np
from jax import lax

D = 512
HID = 512
C_IN = 128
INSTR = 6
HEADS = 8
BLK = 128
LAT = 128
TILE_DEV = 4
NB_DEV = 32
CAP = 4
NBLK = 4096
NTILES = 64
N_TILE = 16


def draw_obs_bias(key, part):
    first_key = jax.random.fold_in(key, 0)
    base_values = jax.random.uniform(first_key, (NBLK, BLK), jnp.float32, -2.0, 2.0)
    return base_values.astype(jnp.bfloat16)


def place_ends(values, own_key, least, top_value):
    index_at = [jax.random.randint(jax.random.fold_in(own_key, axis), (), 0, length) for axis, length in enumerate(values.shape)]
    main_axis = values.shape.index(max(values.shape))
    neighbour = index_at[:main_axis] + [(index_at[main_axis] + 1) % values.shape[main_axis]] + index_at[main_axis + 1:]
    return values.at[tuple(index_at)].set(least).at[tuple(neighbour)].set(top_value)


def steps_of(stream_key, shape, pieces, low, top_value):
    def one(axis_at, blocks):
        steps = jax.random.uniform(jax.random.fold_in(jax.random.fold_in(stream_key, 6), axis_at), (blocks,), jnp.float32, low / len(pieces), top_value / len(pieces))
        return jnp.repeat(jnp.exp(steps), shape[axis_at] // blocks).reshape((-1,) + (1,) * (len(shape) - axis_at - 1))

    gain = one(*pieces[0])
    for cut in pieces[1:]:
        gain = gain * one(*cut)
    return gain


def assign_block(key, own, number, rows, number_of, top, most, slope):
    sequence = jax.random.permutation(key, number_of)
    crowded, common = load_shares(number_of, rows * top, most, slope, True), load_shares(number_of, rows * top, most, slope, False)
    places = jnp.arange(number_of)

    def named(lengths, rotation):
        used = int((lengths > 0).sum())
        fixed = max(1, used // 4)
        passed = fixed + (places - fixed + rotation * (used - fixed)) % max(1, number_of - fixed)
        return jnp.zeros((number_of,), jnp.int32).at[sequence[jnp.where(places < fixed, places, passed)]].set(jnp.asarray(lengths, jnp.int32))

    lengths = jnp.where(number % 4 == 0, named(crowded, number // 4), named(common, number - number // 4 - 1))
    mixed = jax.random.permutation(jax.random.fold_in(own, 3), number_of)
    source_of, sink = mixed[0:number_of // 2 * 2:2], mixed[1:number_of // 2 * 2:2]
    margin = jnp.minimum(lengths[source_of] - 1, most - lengths[sink]) // 2
    margin = jnp.where((source_of == sequence[0]) | (sink == sequence[0]) | (lengths[sink] == 0), 0, jnp.maximum(margin, 0))
    passed = jax.random.randint(jax.random.fold_in(own, 4), (number_of // 2,), 0, 1 << 20) % (margin + 1)
    lengths = lengths.at[source_of].add(-passed).at[sink].add(passed)
    items = jnp.searchsorted(jnp.cumsum(lengths), jnp.arange(rows * top), side="right").astype(jnp.int32)
    grid = items.reshape(top, rows).T
    grid = grid[jax.random.permutation(jax.random.fold_in(own, 1), rows)]
    rotation = jax.random.randint(jax.random.fold_in(own, 2), (rows, 1), 0, top)
    return jnp.take_along_axis(grid, (jnp.arange(top)[None, :] + rotation) % top, axis=1)


def load_shares(number_of, total, limit, lean, full):
    weights = [(1 << 20) // math.isqrt(standing ** lean) + 1 for standing in range(1, number_of + 1)]
    largest = limit if full else min(limit, max(-(-total // number_of), total * weights[0] // sum(weights)))
    least = 1 if total - largest >= number_of - 1 else 0
    holding, spare = [largest] + [least] * (number_of - 1), total - largest - least * (number_of - 1)
    while spare > 0:
        free = [i for i in range(1, number_of) if holding[i] < largest] or [i for i in range(1, number_of) if holding[i] < limit]
        pool, remaining = sum([weights[i] for i in free]), spare
        for i in free:
            addition = min(limit - holding[i], max(1, remaining * weights[i] // pool), spare)
            holding[i] = holding[i] + addition
            spare = spare - addition
    return np.array(holding)


def scatter_about(own_key, extent, deviation, bound, cuts=(), kind=jnp.bfloat16):
    drawn = deviation * jax.random.normal(own_key, extent, jnp.float32)
    if cuts:
        drawn = drawn * steps_of(own_key, extent, cuts, -0.22, 0.18)
    return jnp.clip(drawn, -bound, bound).astype(kind)


def setup_inputs(seed: int = 0) -> dict:
    streams_of = jax.random.split(jax.random.key(seed), 14)
    raw_obs = scatter_about(streams_of[0], (NBLK, BLK, C_IN), 1.0, 6.0, ((0, 128),))
    obs_bias = draw_obs_bias(jax.random.fold_in(streams_of[13], 71), 0)
    instrument = place_ends(jax.random.randint(streams_of[2], (NBLK,), 0, INSTR), jax.random.fold_in(streams_of[2], 1), 0, INSTR - 1).astype(jnp.int32)
    owner_keys = jax.random.split(jax.random.fold_in(streams_of[3], 1), NBLK // NB_DEV)
    owner_turns = jax.random.permutation(jax.random.fold_in(streams_of[3], 3), NBLK // NB_DEV)
    owner = jax.vmap(lambda own, number: assign_block(jax.random.fold_in(streams_of[3], 2), own, number, NB_DEV, N_TILE, 1, CAP, 2))(owner_keys, owner_turns).reshape((NBLK, 1))
    local_tile = place_ends(jax.random.randint(streams_of[4], (NBLK,), 0, TILE_DEV), jax.random.fold_in(streams_of[4], 1), 0, TILE_DEV - 1).astype(jnp.int32)
    latents = scatter_about(streams_of[5], (NTILES * LAT, D), 1.0, 6.0, ((0, 16),))
    first_weight = scatter_about(streams_of[6], (INSTR, C_IN, HID), C_IN ** -0.5, 0.5)
    second_weight = scatter_about(streams_of[7], (INSTR, HID, D), HID ** -0.5, 0.25)
    query_weight = scatter_about(streams_of[8], (D, D), D ** -0.5, 0.25)
    pair_weight = scatter_about(streams_of[9], (D, 2 * D), D ** -0.5, 0.25)
    self_bias = jnp.clip(jax.random.uniform(streams_of[10], (HEADS,), jnp.float32, 6.0, 9.0), 6.0, 9.0)
    out_weight = scatter_about(streams_of[11], (D, D), D ** -0.5, 0.25, ((1, 8),))
    edge_gain = jnp.clip(jnp.exp(math.log(0.4) - 1.3862944 * jax.random.uniform(streams_of[12], (D,), jnp.float32) ** steps_of(streams_of[12], (D,), ((0, 8),), -0.2, 0.2)), 0.1, 0.4)
    return dict(raw_obs=raw_obs, obs_bias=obs_bias, instrument=instrument, owner=owner, local_tile=local_tile, latents=latents, first_weight=first_weight, second_weight=second_weight, query_weight=query_weight, pair_weight=pair_weight, self_bias=self_bias, out_weight=out_weight, edge_gain=edge_gain)


NEG_FLOOR = -1.0e30


def encode_group(raw_rows, kinds, first_weight, second_weight):
    first_sel = jnp.take(first_weight, kinds, axis=0).astype(jnp.float32)
    hidden = jax.nn.silu(jnp.einsum('bnc,bch->bnh', raw_rows.astype(jnp.float32), first_sel)).astype(jnp.bfloat16)
    second_sel = jnp.take(second_weight, kinds, axis=0).astype(jnp.float32)
    return jnp.einsum('bnh,bhd->bnd', hidden.astype(jnp.float32), second_sel).astype(jnp.bfloat16)


def partial_block(queries, key_block, value_block, bias_block, is_filled):
    score_scale = queries.shape[-1] ** -0.5
    scores = jnp.einsum('lhe,bhe->lhb', queries.astype(jnp.float32), key_block.astype(jnp.float32)) * score_scale
    scores = scores + bias_block.astype(jnp.float32)[None, None, :]
    peak_score = jnp.where(is_filled, jnp.max(scores, axis=-1), NEG_FLOOR)
    weights = jnp.where(is_filled, jnp.exp(scores - peak_score[..., None]), 0.0)
    weight_sum = jnp.sum(weights, axis=-1)
    rounded_weights = weights.astype(jnp.bfloat16)
    mixture = jnp.einsum('lhb,bhe->lhe', rounded_weights.astype(jnp.float32), value_block.astype(jnp.float32))
    return peak_score, weight_sum, mixture.reshape(mixture.shape[0], -1)


def combine(left_part, right_part):
    left_peak, left_sum, left_mix = left_part
    right_peak, right_sum, right_mix = right_part
    peak_score = jnp.maximum(left_peak, right_peak)
    left_factor = jnp.exp(left_peak - peak_score)
    right_factor = jnp.exp(right_peak - peak_score)
    weight_sum = left_sum * left_factor + right_sum * right_factor
    mix_shape = left_mix.shape
    head_count = left_peak.shape[-1]
    split_shape = mix_shape[:-1] + (head_count, mix_shape[-1] // head_count)
    mixture = left_mix.reshape(split_shape) * left_factor[..., None] + right_mix.reshape(split_shape) * right_factor[..., None]
    return peak_score, weight_sum, mixture.reshape(mix_shape)


def reference(raw_obs, obs_bias, instrument, owner, local_tile, latents, first_weight, second_weight, query_weight, pair_weight, self_bias, out_weight, edge_gain):
    model_width = latents.shape[1]
    head_count = self_bias.shape[0]
    head_depth = model_width // head_count
    tile_total = latents.shape[0] // LAT
    queries = jnp.dot(latents, query_weight, preferred_element_type=jnp.float32).astype(jnp.bfloat16)
    queries = queries.reshape(tile_total, LAT, head_count, head_depth)
    target = (owner[:, 0] * TILE_DEV + local_tile).astype(jnp.int32)
    group_count = raw_obs.shape[0] // NB_DEV
    raw_groups = raw_obs.reshape(group_count, NB_DEV, BLK, -1)
    bias_groups = obs_bias.reshape(group_count, NB_DEV, BLK)
    kind_groups = instrument.reshape(group_count, NB_DEV)
    target_groups = target.reshape(group_count, NB_DEV)
    initial = (jnp.full((tile_total, LAT, head_count), NEG_FLOOR, jnp.float32),
               jnp.zeros((tile_total, LAT, head_count), jnp.float32),
               jnp.zeros((tile_total, LAT, model_width), jnp.float32))

    def per_group(carry, inputs):
        raw_rows, bias_rows, kinds, target_tiles = inputs
        encoded = encode_group(raw_rows, kinds, first_weight, second_weight)
        projected = jnp.dot(encoded.reshape(-1, model_width), pair_weight, preferred_element_type=jnp.float32).astype(jnp.bfloat16)
        projected = projected.reshape(NB_DEV, BLK, 2, head_count, head_depth)

        def visit(block_index, partial_state):
            tile_place = target_tiles[block_index]
            block_part = partial_block(queries[tile_place], projected[block_index, :, 0], projected[block_index, :, 1], bias_rows[block_index], True)
            current = tuple(lax.dynamic_index_in_dim(buffer, tile_place, 0, False) for buffer in partial_state)
            merged = combine(current, block_part)
            return tuple(lax.dynamic_update_index_in_dim(buffer, replacement, tile_place, 0) for buffer, replacement in zip(partial_state, merged))

        return lax.fori_loop(0, NB_DEV, visit, carry), None

    partial_state, leftover = lax.scan(per_group, initial, (raw_groups, bias_groups, kind_groups, target_groups))
    self_pair = jnp.dot(latents, pair_weight, preferred_element_type=jnp.float32).astype(jnp.bfloat16)
    self_pair = self_pair.reshape(tile_total, LAT, 2, head_count, head_depth)
    self_score = jnp.sum(queries.astype(jnp.float32) * self_pair[:, :, 0].astype(jnp.float32), axis=-1) * (head_depth ** -0.5) + self_bias
    self_part = (self_score, jnp.ones_like(self_score), self_pair[:, :, 1].astype(jnp.float32).reshape(tile_total, LAT, model_width))
    peak_score, weight_sum, mixture = combine(partial_state, self_part)
    attended = (mixture.reshape(tile_total, LAT, head_count, head_depth) / weight_sum[..., None]).reshape(tile_total * LAT, model_width).astype(jnp.bfloat16)
    updated = latents.astype(jnp.float32) + jnp.dot(attended, out_weight, preferred_element_type=jnp.float32)
    before = jnp.roll(updated, 1, axis=0)
    after = jnp.roll(updated, -1, axis=0)
    return updated + edge_gain[None, :] * (before + after - 2.0 * updated)
```

```python
import functools

import jax
import jax.numpy as jnp
from jax import lax
from jax.experimental import pallas as pl
from jax.experimental.pallas import tpu as pltpu
from jax.sharding import PartitionSpec as P

TILE_DEV = 4
NEG_FLOOR = -1e30
INTERPRET = False


def extended(cells, sides, width):
    for axis, dim in sides:
        count = lax.axis_size(axis)
        head = lax.slice_in_dim(cells, 0, width, axis=dim)
        tail = lax.slice_in_dim(cells, cells.shape[dim] - width, cells.shape[dim], axis=dim)
        cells = jnp.concatenate(
            [
                lax.ppermute(tail, axis, [(i, (i + 1) % count) for i in range(count)]),
                cells,
                lax.ppermute(head, axis, [((i + 1) % count, i) for i in range(count)]),
            ],
            axis=dim,
        )
    return cells


def attend_kernel(kind_ref, tile_ref, raw_ref, bias_ref, w1_ref, w2_ref, pair_ref, q_ref,
                  m_ref, l_ref, acc_ref, enc_ref, *, heads, depth):
    slot = pl.program_id(0)

    @pl.when(slot == 0)
    def _():
        m_ref[...] = jnp.full(m_ref.shape, NEG_FLOOR, jnp.float32)
        l_ref[...] = jnp.zeros(l_ref.shape, jnp.float32)
        acc_ref[...] = jnp.zeros(acc_ref.shape, jnp.float32)

    tile = tile_ref[slot]
    kind = kind_ref[slot]
    width = heads * depth
    for k in range(w1_ref.shape[0]):
        @pl.when((tile >= 0) & (kind == k))
        def _():
            pre = jnp.dot(raw_ref[0], w1_ref[k], preferred_element_type=jnp.float32)
            hidden = (pre / (1.0 + jnp.exp(-pre))).astype(jnp.bfloat16)
            enc_ref[...] = jnp.dot(hidden, w2_ref[k], preferred_element_type=jnp.float32).astype(jnp.bfloat16)

    for j in range(q_ref.shape[0]):
        @pl.when(tile == j)
        def _():
            pair = jnp.dot(enc_ref[...], pair_ref[...], preferred_element_type=jnp.float32).astype(jnp.bfloat16)
            queries = q_ref[j]
            bias = bias_ref[0, 0:1, :].astype(jnp.float32)
            scale = depth ** (-0.5)
            for h in range(heads):
                cols = slice(h * depth, (h + 1) * depth)
                scores = lax.dot_general(
                    queries[:, cols], pair[:, cols], (((1,), (1,)), ((), ())),
                    preferred_element_type=jnp.float32,
                ) * scale + bias
                peak = jnp.max(scores, axis=1, keepdims=True)
                weights = jnp.exp(scores - peak)
                weight_sum = jnp.sum(weights, axis=1, keepdims=True)
                mixture = jnp.dot(
                    weights.astype(jnp.bfloat16), pair[:, width + h * depth:width + (h + 1) * depth],
                    preferred_element_type=jnp.float32,
                )
                old_peak = m_ref[j, :, h:h + 1]
                new_peak = jnp.maximum(old_peak, peak)
                old_factor = jnp.exp(old_peak - new_peak)
                new_factor = jnp.exp(peak - new_peak)
                m_ref[j, :, h:h + 1] = new_peak
                l_ref[j, :, h:h + 1] = l_ref[j, :, h:h + 1] * old_factor + weight_sum * new_factor
                acc_ref[j, :, cols] = acc_ref[j, :, cols] * old_factor + mixture * new_factor


def attend_slots(kinds, tiles, packed, block_rows, first_weight, second_weight, pair_weight, queries, heads):
    slots, _, chans = packed.shape
    tiles_here, latent_rows, width = queries.shape
    depth = width // heads
    const3 = lambda s: (0, 0, 0)
    const2 = lambda s: (0, 0)
    smem = pl.BlockSpec(memory_space=pltpu.SMEM)
    flops = slots * 2 * block_rows * (chans * first_weight.shape[2] + first_weight.shape[2] * width
                                      + width * 2 * width + 2 * latent_rows * width)
    return pl.pallas_call(
        functools.partial(attend_kernel, heads=heads, depth=depth),
        grid=(slots,),
        in_specs=[
            smem,
            smem,
            pl.BlockSpec((1, block_rows, chans), lambda s: (s, 0, 0)),
            pl.BlockSpec((1, 8, chans), lambda s: (s, block_rows // 8, 0)),
            pl.BlockSpec(first_weight.shape, const3),
            pl.BlockSpec(second_weight.shape, const3),
            pl.BlockSpec(pair_weight.shape, const2),
            pl.BlockSpec(queries.shape, const3),
        ],
        out_specs=[
            pl.BlockSpec((tiles_here, latent_rows, heads), const3),
            pl.BlockSpec((tiles_here, latent_rows, heads), const3),
            pl.BlockSpec((tiles_here, latent_rows, width), const3),
        ],
        out_shape=[
            jax.ShapeDtypeStruct((tiles_here, latent_rows, heads), jnp.float32),
            jax.ShapeDtypeStruct((tiles_here, latent_rows, heads), jnp.float32),
            jax.ShapeDtypeStruct((tiles_here, latent_rows, width), jnp.float32),
        ],
        scratch_shapes=[pltpu.VMEM((block_rows, width), jnp.bfloat16)],
        compiler_params=pltpu.CompilerParams(dimension_semantics=("arbitrary",)),
        cost_estimate=pl.CostEstimate(
            flops=int(flops), transcendentals=int(slots * block_rows * (first_weight.shape[2] + heads * latent_rows)),
            bytes_accessed=int(packed.size * 2 + first_weight.size * 2 + second_weight.size * 2
                               + pair_weight.size * 2 + queries.size * 2 + tiles_here * latent_rows * (width + 2 * heads) * 4),
        ),
        interpret=INTERPRET,
    )(kinds, tiles, packed, packed, first_weight, second_weight, pair_weight, queries)


def local(
    raw_obs,
    obs_bias,
    instrument,
    owner,
    local_tile,
    latents,
    first_weight,
    second_weight,
    query_weight,
    pair_weight,
    self_bias,
    out_weight,
    edge_gain,
):
    blocks, block_rows, chans = raw_obs.shape
    owners = lax.axis_size("tile")
    obs_count = lax.axis_size("obs")
    model_width = latents.shape[1]
    head_count = self_bias.shape[0]
    head_depth = model_width // head_count
    tiles_here = TILE_DEV
    slots_each = max(2, 2 * blocks // owners)
    slot_total = owners * slots_each

    targets = owner[:, 0]
    member = (targets[:, None] == jnp.arange(owners, dtype=jnp.int32)[None, :]).astype(jnp.int32)
    slot_rank = jnp.sum(jnp.cumsum(member, axis=0) * member, axis=1) - 1
    position = targets * slots_each + slot_rank
    select = (position[None, :] == jnp.arange(slot_total, dtype=jnp.int32)[:, None]).astype(jnp.bfloat16)
    lane = jnp.arange(chans, dtype=jnp.int32)[None, :]
    tag_row = jnp.where(lane == 0, (local_tile + 1)[:, None], jnp.where(lane == 1, instrument[:, None], 0))
    packed = jnp.concatenate(
        [
            raw_obs,
            obs_bias[:, None, :],
            tag_row[:, None, :].astype(jnp.bfloat16),
            jnp.zeros((blocks, 6, chans), jnp.bfloat16),
        ],
        axis=1,
    )
    placed = jnp.dot(select, packed.reshape(blocks, -1), preferred_element_type=jnp.float32)
    placed = placed.astype(jnp.bfloat16).reshape((slot_total,) + packed.shape[1:])
    received = lax.all_to_all(placed, "tile", split_axis=0, concat_axis=0, tiled=True)
    slot_tags = received[:, block_rows + 1, 0:2].astype(jnp.float32).astype(jnp.int32)
    slot_tiles = slot_tags[:, 0] - 1
    slot_kinds = slot_tags[:, 1]

    queries = jnp.dot(latents, query_weight, preferred_element_type=jnp.float32).astype(jnp.bfloat16)
    part_peak, part_sum, part_mix = attend_slots(
        slot_kinds, slot_tiles, received, block_rows, first_weight, second_weight, pair_weight,
        queries.reshape(tiles_here, -1, model_width), head_count,
    )

    row_total = latents.shape[0]
    share = row_total // obs_count
    partials = jnp.concatenate(
        [
            part_mix.reshape(row_total, model_width),
            part_peak.reshape(row_total, head_count),
            part_sum.reshape(row_total, head_count),
        ],
        axis=1,
    )
    mine = lax.all_to_all(partials, "obs", split_axis=0, concat_axis=0, tiled=True)
    mine = mine.reshape(obs_count, share, model_width + 2 * head_count)
    mix_o = mine[..., :model_width].reshape(obs_count, share, head_count, head_depth)
    peak_o = mine[..., model_width:model_width + head_count]
    sum_o = mine[..., model_width + head_count:]

    row_start = lax.axis_index("obs") * share
    latent_mine = lax.dynamic_slice_in_dim(latents, row_start, share, 0)
    query_mine = lax.dynamic_slice_in_dim(queries, row_start, share, 0).reshape(share, head_count, head_depth)
    self_pair = jnp.dot(latent_mine, pair_weight, preferred_element_type=jnp.float32).astype(jnp.bfloat16)
    self_keys = self_pair[:, :model_width].reshape(share, head_count, head_depth)
    self_values = self_pair[:, model_width:].reshape(share, head_count, head_depth)
    self_score = (
        jnp.sum(query_mine.astype(jnp.float32) * self_keys.astype(jnp.float32), axis=-1)
        * head_depth ** (-0.5)
        + self_bias
    )
    peak = jnp.maximum(jnp.max(peak_o, axis=0), self_score)
    factor_o = jnp.exp(peak_o - peak[None])
    factor_s = jnp.exp(self_score - peak)
    total = factor_s + jnp.sum(factor_o * sum_o, axis=0)
    mixture = factor_s[..., None] * self_values.astype(jnp.float32) + jnp.sum(
        factor_o[..., None] * mix_o, axis=0
    )
    attended = (mixture / total[..., None]).reshape(share, model_width).astype(jnp.bfloat16)
    attended = lax.all_gather(attended, "obs", axis=0, tiled=True)

    column_count = out_weight.shape[1]
    column_start = lax.axis_index("obs") * column_count
    latent_columns = lax.dynamic_slice_in_dim(latents, column_start, column_count, 1).astype(
        jnp.float32
    )
    updated = latent_columns + jnp.dot(attended, out_weight, preferred_element_type=jnp.float32)
    padded = extended(updated, (("tile", 0),), 1)
    return updated + edge_gain[None, :] * (padded[:-2] + padded[2:] - 2.0 * updated)


def solution(mesh):
    return jax.shard_map(
        local,
        mesh=mesh,
        in_specs=(
            P(("obs", "tile"), None, None),
            P(("obs", "tile"), None),
            P(("obs", "tile")),
            P(("obs", "tile"), None),
            P(("obs", "tile")),
            P("tile", None),
            P(),
            P(),
            P(),
            P(),
            P(),
            P(None, "obs"),
            P("obs"),
        ),
        out_specs=P("tile", "obs"),
        check_vma=False,
    )
```

```python
import functools

import jax
import jax.numpy as jnp
from jax import lax
from jax.experimental import pallas as pl
from jax.experimental.pallas import tpu as pltpu
from jax.sharding import PartitionSpec as P

TILE_DEV = 4
NEG_FLOOR = -1e30
INTERPRET = False


def extended(cells, sides, width):
    for axis, dim in sides:
        count = lax.axis_size(axis)
        head = lax.slice_in_dim(cells, 0, width, axis=dim)
        tail = lax.slice_in_dim(cells, cells.shape[dim] - width, cells.shape[dim], axis=dim)
        cells = jnp.concatenate(
            [
                lax.ppermute(tail, axis, [(i, (i + 1) % count) for i in range(count)]),
                cells,
                lax.ppermute(head, axis, [((i + 1) % count, i) for i in range(count)]),
            ],
            axis=dim,
        )
    return cells


def attend_kernel(kind_ref, tile_ref, raw_ref, bias_ref, w1_ref, w2_ref, kwt_ref, vw_ref, q_ref,
                  m_ref, l_ref, acc_ref, enc_ref, qs_ref, kbd_ref, vbd_ref, p_ref, *, heads, depth):
    slot = pl.program_id(0)

    @pl.when(slot == 0)
    def _():
        m_ref[...] = jnp.full(m_ref.shape, NEG_FLOOR, jnp.float32)
        l_ref[...] = jnp.zeros(l_ref.shape, jnp.float32)
        acc_ref[...] = jnp.zeros(acc_ref.shape, jnp.float32)

    tile = tile_ref[slot]
    kind = kind_ref[slot]
    width = heads * depth
    block_rows = enc_ref.shape[0]
    for k in range(w1_ref.shape[0]):
        @pl.when((tile >= 0) & (kind == k))
        def _():
            pre = jnp.dot(raw_ref[0], w1_ref[k], preferred_element_type=jnp.float32)
            hidden = (pre / (1.0 + jnp.exp(-pre))).astype(jnp.bfloat16)
            enc_ref[...] = jnp.dot(hidden, w2_ref[k], preferred_element_type=jnp.float32).astype(jnp.bfloat16)

    for j in range(q_ref.shape[0]):
        @pl.when(tile == j)
        def _():
            qs_ref[...] = q_ref[j]

    @pl.when(tile >= 0)
    def _():
        encoded = enc_ref[...]
        keys_t = lax.dot_general(
            kwt_ref[...], encoded, (((1,), (1,)), ((), ())), preferred_element_type=jnp.float32
        ).astype(jnp.bfloat16)
        values = jnp.dot(encoded, vw_ref[...], preferred_element_type=jnp.float32).astype(jnp.bfloat16)
        feature_row = lax.broadcasted_iota(jnp.int32, keys_t.shape, 0)
        feature_col = lax.broadcasted_iota(jnp.int32, values.shape, 1)
        for h in range(heads):
            rows = slice(h * block_rows, (h + 1) * block_rows)
            kbd_ref[:, rows] = jnp.where(
                (feature_row >= h * depth) & (feature_row < (h + 1) * depth), keys_t, jnp.zeros_like(keys_t)
            )
            vbd_ref[rows, :] = jnp.where(
                (feature_col >= h * depth) & (feature_col < (h + 1) * depth), values, jnp.zeros_like(values)
            )
        scores = jnp.dot(qs_ref[...], kbd_ref[...], preferred_element_type=jnp.float32)
        bias = bias_ref[0, 0:1, :].astype(jnp.float32)
        scale = depth ** (-0.5)
        peaks, sums = [], []
        for h in range(heads):
            rows = slice(h * block_rows, (h + 1) * block_rows)
            head_scores = scores[:, rows] * scale + bias
            peak = jnp.max(head_scores, axis=1, keepdims=True)
            weights = jnp.exp(head_scores - peak)
            peaks.append(peak)
            sums.append(jnp.sum(weights, axis=1, keepdims=True))
            p_ref[:, rows] = weights.astype(jnp.bfloat16)
        mixture = jnp.dot(p_ref[...], vbd_ref[...], preferred_element_type=jnp.float32)
        for j in range(q_ref.shape[0]):
            @pl.when(tile == j)
            def _():
                for h in range(heads):
                    cols = slice(h * depth, (h + 1) * depth)
                    old_peak = m_ref[j, :, h:h + 1]
                    new_peak = jnp.maximum(old_peak, peaks[h])
                    old_factor = jnp.exp(old_peak - new_peak)
                    new_factor = jnp.exp(peaks[h] - new_peak)
                    m_ref[j, :, h:h + 1] = new_peak
                    l_ref[j, :, h:h + 1] = l_ref[j, :, h:h + 1] * old_factor + sums[h] * new_factor
                    acc_ref[j, :, cols] = acc_ref[j, :, cols] * old_factor + mixture[:, cols] * new_factor


def attend_slots(kinds, tiles, packed, block_rows, first_weight, second_weight, pair_weight, queries, heads):
    slots, _, chans = packed.shape
    tiles_here, latent_rows, width = queries.shape
    depth = width // heads
    key_weight_t = pair_weight[:, :width].T
    value_weight = pair_weight[:, width:]
    const3 = lambda s: (0, 0, 0)
    const2 = lambda s: (0, 0)
    smem = pl.BlockSpec(memory_space=pltpu.SMEM)
    flops = slots * 2 * block_rows * (chans * first_weight.shape[2] + first_weight.shape[2] * width
                                      + width * 2 * width + 2 * latent_rows * width * heads)
    return pl.pallas_call(
        functools.partial(attend_kernel, heads=heads, depth=depth),
        grid=(slots,),
        in_specs=[
            smem,
            smem,
            pl.BlockSpec((1, block_rows, chans), lambda s: (s, 0, 0)),
            pl.BlockSpec((1, 8, chans), lambda s: (s, block_rows // 8, 0)),
            pl.BlockSpec(first_weight.shape, const3),
            pl.BlockSpec(second_weight.shape, const3),
            pl.BlockSpec(key_weight_t.shape, const2),
            pl.BlockSpec(value_weight.shape, const2),
            pl.BlockSpec(queries.shape, const3),
        ],
        out_specs=[
            pl.BlockSpec((tiles_here, latent_rows, heads), const3),
            pl.BlockSpec((tiles_here, latent_rows, heads), const3),
            pl.BlockSpec((tiles_here, latent_rows, width), const3),
        ],
        out_shape=[
            jax.ShapeDtypeStruct((tiles_here, latent_rows, heads), jnp.float32),
            jax.ShapeDtypeStruct((tiles_here, latent_rows, heads), jnp.float32),
            jax.ShapeDtypeStruct((tiles_here, latent_rows, width), jnp.float32),
        ],
        scratch_shapes=[
            pltpu.VMEM((block_rows, width), jnp.bfloat16),
            pltpu.VMEM((latent_rows, width), jnp.bfloat16),
            pltpu.VMEM((width, heads * block_rows), jnp.bfloat16),
            pltpu.VMEM((heads * block_rows, width), jnp.bfloat16),
            pltpu.VMEM((latent_rows, heads * block_rows), jnp.bfloat16),
        ],
        compiler_params=pltpu.CompilerParams(dimension_semantics=("arbitrary",)),
        cost_estimate=pl.CostEstimate(
            flops=int(flops), transcendentals=int(slots * block_rows * (first_weight.shape[2] + heads * latent_rows)),
            bytes_accessed=int(packed.size * 2 + first_weight.size * 2 + second_weight.size * 2
                               + pair_weight.size * 2 + queries.size * 2 + tiles_here * latent_rows * (width + 2 * heads) * 4),
        ),
        interpret=INTERPRET,
    )(kinds, tiles, packed, packed, first_weight, second_weight, key_weight_t, value_weight, queries)


def local(
    raw_obs,
    obs_bias,
    instrument,
    owner,
    local_tile,
    latents,
    first_weight,
    second_weight,
    query_weight,
    pair_weight,
    self_bias,
    out_weight,
    edge_gain,
):
    blocks, block_rows, chans = raw_obs.shape
    owners = lax.axis_size("tile")
    obs_count = lax.axis_size("obs")
    model_width = latents.shape[1]
    head_count = self_bias.shape[0]
    head_depth = model_width // head_count
    tiles_here = TILE_DEV
    slots_each = max(2, 2 * blocks // owners)
    slot_total = owners * slots_each

    targets = owner[:, 0]
    member = (targets[:, None] == jnp.arange(owners, dtype=jnp.int32)[None, :]).astype(jnp.int32)
    slot_rank = jnp.sum(jnp.cumsum(member, axis=0) * member, axis=1) - 1
    position = targets * slots_each + slot_rank
    select = (position[None, :] == jnp.arange(slot_total, dtype=jnp.int32)[:, None]).astype(jnp.bfloat16)
    lane = jnp.arange(chans, dtype=jnp.int32)[None, :]
    tag_row = jnp.where(lane == 0, (local_tile + 1)[:, None], jnp.where(lane == 1, instrument[:, None], 0))
    packed = jnp.concatenate(
        [
            raw_obs,
            obs_bias[:, None, :],
            tag_row[:, None, :].astype(jnp.bfloat16),
            jnp.zeros((blocks, 6, chans), jnp.bfloat16),
        ],
        axis=1,
    )
    placed = jnp.dot(select, packed.reshape(blocks, -1), preferred_element_type=jnp.float32)
    placed = placed.astype(jnp.bfloat16).reshape((slot_total,) + packed.shape[1:])
    received = lax.all_to_all(placed, "tile", split_axis=0, concat_axis=0, tiled=True)
    slot_tags = received[:, block_rows + 1, 0:2].astype(jnp.float32).astype(jnp.int32)
    slot_tiles = slot_tags[:, 0] - 1
    slot_kinds = slot_tags[:, 1]

    queries = jnp.dot(latents, query_weight, preferred_element_type=jnp.float32).astype(jnp.bfloat16)
    part_peak, part_sum, part_mix = attend_slots(
        slot_kinds, slot_tiles, received, block_rows, first_weight, second_weight, pair_weight,
        queries.reshape(tiles_here, -1, model_width), head_count,
    )

    row_total = latents.shape[0]
    share = row_total // obs_count
    partials = jnp.concatenate(
        [
            part_mix.reshape(row_total, model_width),
            part_peak.reshape(row_total, head_count),
            part_sum.reshape(row_total, head_count),
        ],
        axis=1,
    )
    mine = lax.all_to_all(partials, "obs", split_axis=0, concat_axis=0, tiled=True)
    mine = mine.reshape(obs_count, share, model_width + 2 * head_count)
    mix_o = mine[..., :model_width].reshape(obs_count, share, head_count, head_depth)
    peak_o = mine[..., model_width:model_width + head_count]
    sum_o = mine[..., model_width + head_count:]

    row_start = lax.axis_index("obs") * share
    latent_mine = lax.dynamic_slice_in_dim(latents, row_start, share, 0)
    query_mine = lax.dynamic_slice_in_dim(queries, row_start, share, 0).reshape(share, head_count, head_depth)
    self_pair = jnp.dot(latent_mine, pair_weight, preferred_element_type=jnp.float32).astype(jnp.bfloat16)
    self_keys = self_pair[:, :model_width].reshape(share, head_count, head_depth)
    self_values = self_pair[:, model_width:].reshape(share, head_count, head_depth)
    self_score = (
        jnp.sum(query_mine.astype(jnp.float32) * self_keys.astype(jnp.float32), axis=-1)
        * head_depth ** (-0.5)
        + self_bias
    )
    peak = jnp.maximum(jnp.max(peak_o, axis=0), self_score)
    factor_o = jnp.exp(peak_o - peak[None])
    factor_s = jnp.exp(self_score - peak)
    total = factor_s + jnp.sum(factor_o * sum_o, axis=0)
    mixture = factor_s[..., None] * self_values.astype(jnp.float32) + jnp.sum(
        factor_o[..., None] * mix_o, axis=0
    )
    attended = (mixture / total[..., None]).reshape(share, model_width).astype(jnp.bfloat16)
    attended = lax.all_gather(attended, "obs", axis=0, tiled=True)

    column_count = out_weight.shape[1]
    column_start = lax.axis_index("obs") * column_count
    latent_columns = lax.dynamic_slice_in_dim(latents, column_start, column_count, 1).astype(
        jnp.float32
    )
    updated = latent_columns + jnp.dot(attended, out_weight, preferred_element_type=jnp.float32)
    padded = extended(updated, (("tile", 0),), 1)
    return updated + edge_gain[None, :] * (padded[:-2] + padded[2:] - 2.0 * updated)


def solution(mesh):
    return jax.shard_map(
        local,
        mesh=mesh,
        in_specs=(
            P(("obs", "tile"), None, None),
            P(("obs", "tile"), None),
            P(("obs", "tile")),
            P(("obs", "tile"), None),
            P(("obs", "tile")),
            P("tile", None),
            P(),
            P(),
            P(),
            P(),
            P(),
            P(None, "obs"),
            P("obs"),
        ),
        out_specs=P("tile", "obs"),
        check_vma=False,
    )
```

```python
import functools

import jax
import jax.numpy as jnp
from jax import lax
from jax.experimental import pallas as pl
from jax.experimental.pallas import tpu as pltpu
from jax.sharding import PartitionSpec as P

TILE_DEV = 4
NEG_FLOOR = -1e30
INTERPRET = False


def extended(cells, sides, width):
    for axis, dim in sides:
        count = lax.axis_size(axis)
        head = lax.slice_in_dim(cells, 0, width, axis=dim)
        tail = lax.slice_in_dim(cells, cells.shape[dim] - width, cells.shape[dim], axis=dim)
        cells = jnp.concatenate(
            [
                lax.ppermute(tail, axis, [(i, (i + 1) % count) for i in range(count)]),
                cells,
                lax.ppermute(head, axis, [((i + 1) % count, i) for i in range(count)]),
            ],
            axis=dim,
        )
    return cells


def attend_kernel(kind_ref, tile_ref, raw_ref, bias_ref, w1_ref, w2_ref, kwt_ref, vw_ref, q_ref,
                  m_ref, l_ref, acc_ref, enc_ref, qs_ref, kbd_ref, vbd_ref, p_ref, *, heads, depth):
    slot = pl.program_id(0)

    @pl.when(slot == 0)
    def _():
        m_ref[...] = jnp.full(m_ref.shape, NEG_FLOOR, jnp.float32)
        l_ref[...] = jnp.zeros(l_ref.shape, jnp.float32)
        acc_ref[...] = jnp.zeros(acc_ref.shape, jnp.float32)

    tile = tile_ref[slot]
    kind = kind_ref[slot]
    width = heads * depth
    block_rows = enc_ref.shape[0]
    for k in range(w1_ref.shape[0]):
        @pl.when((tile >= 0) & (kind == k))
        def _():
            pre = jnp.dot(raw_ref[0], w1_ref[k], preferred_element_type=jnp.float32)
            hidden = (pre / (1.0 + jnp.exp(-pre))).astype(jnp.bfloat16)
            enc_ref[...] = jnp.dot(hidden, w2_ref[k], preferred_element_type=jnp.float32).astype(jnp.bfloat16)

    for j in range(q_ref.shape[0]):
        @pl.when(tile == j)
        def _():
            qs_ref[...] = q_ref[j]

    @pl.when(tile >= 0)
    def _():
        encoded = enc_ref[...]
        keys_t = lax.dot_general(
            kwt_ref[...], encoded, (((1,), (1,)), ((), ())), preferred_element_type=jnp.float32
        ).astype(jnp.bfloat16)
        values = jnp.dot(encoded, vw_ref[...], preferred_element_type=jnp.float32).astype(jnp.bfloat16)
        feature_row = lax.broadcasted_iota(jnp.int32, keys_t.shape, 0)
        feature_col = lax.broadcasted_iota(jnp.int32, values.shape, 1)
        for h in range(heads):
            rows = slice(h * block_rows, (h + 1) * block_rows)
            kbd_ref[:, rows] = jnp.where(
                (feature_row >= h * depth) & (feature_row < (h + 1) * depth), keys_t, jnp.zeros_like(keys_t)
            )
            vbd_ref[rows, :] = jnp.where(
                (feature_col >= h * depth) & (feature_col < (h + 1) * depth), values, jnp.zeros_like(values)
            )
        scores = jnp.dot(qs_ref[...], kbd_ref[...], preferred_element_type=jnp.float32)
        bias = bias_ref[0, 0:1, :].astype(jnp.float32)
        scale = depth ** (-0.5)
        peaks, sums = [], []
        for h in range(heads):
            rows = slice(h * block_rows, (h + 1) * block_rows)
            head_scores = scores[:, rows] * scale + bias
            peak = jnp.max(head_scores, axis=1, keepdims=True)
            weights = jnp.exp(head_scores - peak)
            peaks.append(peak)
            sums.append(jnp.sum(weights, axis=1, keepdims=True))
            p_ref[:, rows] = weights.astype(jnp.bfloat16)
        mixture = jnp.dot(p_ref[...], vbd_ref[...], preferred_element_type=jnp.float32)
        for j in range(q_ref.shape[0]):
            @pl.when(tile == j)
            def _():
                for h in range(heads):
                    cols = slice(h * depth, (h + 1) * depth)
                    old_peak = m_ref[j, :, h:h + 1]
                    new_peak = jnp.maximum(old_peak, peaks[h])
                    old_factor = jnp.exp(old_peak - new_peak)
                    new_factor = jnp.exp(peaks[h] - new_peak)
                    m_ref[j, :, h:h + 1] = new_peak
                    l_ref[j, :, h:h + 1] = l_ref[j, :, h:h + 1] * old_factor + sums[h] * new_factor
                    acc_ref[j, :, cols] = acc_ref[j, :, cols] * old_factor + mixture[:, cols] * new_factor


def attend_slots(kinds, tiles, packed, block_rows, first_weight, second_weight, pair_weight, queries, heads):
    slots, _, chans = packed.shape
    tiles_here, latent_rows, width = queries.shape
    depth = width // heads
    key_weight_t = pair_weight[:, :width].T
    value_weight = pair_weight[:, width:]
    const3 = lambda s: (0, 0, 0)
    const2 = lambda s: (0, 0)
    smem = pl.BlockSpec(memory_space=pltpu.SMEM)
    flops = slots * 2 * block_rows * (chans * first_weight.shape[2] + first_weight.shape[2] * width
                                      + width * 2 * width + 2 * latent_rows * width * heads)
    return pl.pallas_call(
        functools.partial(attend_kernel, heads=heads, depth=depth),
        grid=(slots,),
        in_specs=[
            smem,
            smem,
            pl.BlockSpec((1, block_rows, chans), lambda s: (s, 0, 0)),
            pl.BlockSpec((1, 8, chans), lambda s: (s, block_rows // 8, 0)),
            pl.BlockSpec(first_weight.shape, const3),
            pl.BlockSpec(second_weight.shape, const3),
            pl.BlockSpec(key_weight_t.shape, const2),
            pl.BlockSpec(value_weight.shape, const2),
            pl.BlockSpec(queries.shape, const3),
        ],
        out_specs=[
            pl.BlockSpec((tiles_here, latent_rows, heads), const3),
            pl.BlockSpec((tiles_here, latent_rows, heads), const3),
            pl.BlockSpec((tiles_here, latent_rows, width), const3),
        ],
        out_shape=[
            jax.ShapeDtypeStruct((tiles_here, latent_rows, heads), jnp.float32),
            jax.ShapeDtypeStruct((tiles_here, latent_rows, heads), jnp.float32),
            jax.ShapeDtypeStruct((tiles_here, latent_rows, width), jnp.float32),
        ],
        scratch_shapes=[
            pltpu.VMEM((block_rows, width), jnp.bfloat16),
            pltpu.VMEM((latent_rows, width), jnp.bfloat16),
            pltpu.VMEM((width, heads * block_rows), jnp.bfloat16),
            pltpu.VMEM((heads * block_rows, width), jnp.bfloat16),
            pltpu.VMEM((latent_rows, heads * block_rows), jnp.bfloat16),
        ],
        compiler_params=pltpu.CompilerParams(dimension_semantics=("arbitrary",)),
        cost_estimate=pl.CostEstimate(
            flops=int(flops), transcendentals=int(slots * block_rows * (first_weight.shape[2] + heads * latent_rows)),
            bytes_accessed=int(packed.size * 2 + first_weight.size * 2 + second_weight.size * 2
                               + pair_weight.size * 2 + queries.size * 2 + tiles_here * latent_rows * (width + 2 * heads) * 4),
        ),
        interpret=INTERPRET,
    )(kinds, tiles, packed, packed, first_weight, second_weight, key_weight_t, value_weight, queries)


def local(
    raw_obs,
    obs_bias,
    instrument,
    owner,
    local_tile,
    latents,
    first_weight,
    second_weight,
    query_weight,
    pair_weight,
    self_bias,
    out_weight,
    edge_gain,
):
    blocks, block_rows, chans = raw_obs.shape
    owners = lax.axis_size("tile")
    obs_count = lax.axis_size("obs")
    model_width = latents.shape[1]
    head_count = self_bias.shape[0]
    head_depth = model_width // head_count
    tiles_here = TILE_DEV
    slots_each = max(2, 2 * blocks // owners)
    slot_total = owners * slots_each

    targets = owner[:, 0]
    member = (targets[:, None] == jnp.arange(owners, dtype=jnp.int32)[None, :]).astype(jnp.int32)
    slot_rank = jnp.sum(jnp.cumsum(member, axis=0) * member, axis=1) - 1
    position = targets * slots_each + slot_rank
    select = (position[None, :] == jnp.arange(slot_total, dtype=jnp.int32)[:, None]).astype(jnp.bfloat16)
    lane = jnp.arange(chans, dtype=jnp.int32)[None, :]
    tag_row = jnp.where(lane == 0, (local_tile + 1)[:, None], jnp.where(lane == 1, instrument[:, None], 0))
    packed = jnp.concatenate(
        [
            raw_obs,
            obs_bias[:, None, :],
            tag_row[:, None, :].astype(jnp.bfloat16),
            jnp.zeros((blocks, 6, chans), jnp.bfloat16),
        ],
        axis=1,
    )
    placed = jnp.dot(select, packed.reshape(blocks, -1), preferred_element_type=jnp.float32)
    placed = placed.astype(jnp.bfloat16).reshape((slot_total,) + packed.shape[1:])
    received = lax.all_to_all(placed, "tile", split_axis=0, concat_axis=0, tiled=True)
    slot_tags = received[:, block_rows + 1, 0:2].astype(jnp.float32).astype(jnp.int32)
    slot_tiles = slot_tags[:, 0] - 1
    slot_kinds = slot_tags[:, 1]

    queries = jnp.dot(latents, query_weight, preferred_element_type=jnp.float32).astype(jnp.bfloat16)
    part_peak, part_sum, part_mix = attend_slots(
        slot_kinds, slot_tiles, received, block_rows, first_weight, second_weight, pair_weight,
        queries.reshape(tiles_here, -1, model_width), head_count,
    )

    row_total = latents.shape[0]
    share = row_total // obs_count
    partials = jnp.concatenate(
        [
            part_mix.reshape(row_total, model_width),
            part_peak.reshape(row_total, head_count),
            part_sum.reshape(row_total, head_count),
        ],
        axis=1,
    )
    mine = lax.all_to_all(partials, "obs", split_axis=0, concat_axis=0, tiled=True)
    mine = mine.reshape(obs_count, share, model_width + 2 * head_count)
    mix_o = mine[..., :model_width].reshape(obs_count, share, head_count, head_depth)
    peak_o = mine[..., model_width:model_width + head_count]
    sum_o = mine[..., model_width + head_count:]

    row_start = lax.axis_index("obs") * share
    latent_mine = lax.dynamic_slice_in_dim(latents, row_start, share, 0)
    query_mine = lax.dynamic_slice_in_dim(queries, row_start, share, 0).reshape(share, head_count, head_depth)
    self_pair = jnp.dot(latent_mine, pair_weight, preferred_element_type=jnp.float32).astype(jnp.bfloat16)
    self_keys = self_pair[:, :model_width].reshape(share, head_count, head_depth)
    self_values = self_pair[:, model_width:].reshape(share, head_count, head_depth)
    self_score = (
        jnp.sum(query_mine.astype(jnp.float32) * self_keys.astype(jnp.float32), axis=-1)
        * head_depth ** (-0.5)
        + self_bias
    )
    peak = jnp.maximum(jnp.max(peak_o, axis=0), self_score)
    factor_o = jnp.exp(peak_o - peak[None])
    factor_s = jnp.exp(self_score - peak)
    total = factor_s + jnp.sum(factor_o * sum_o, axis=0)
    mixture = factor_s[..., None] * self_values.astype(jnp.float32) + jnp.sum(
        factor_o[..., None] * mix_o, axis=0
    )
    attended = (mixture / total[..., None]).reshape(share, model_width).astype(jnp.bfloat16)
    full_out_weight = lax.all_gather(out_weight, "obs", axis=1, tiled=True)
    updated_rows = latent_mine.astype(jnp.float32) + jnp.dot(
        attended, full_out_weight, preferred_element_type=jnp.float32
    )
    updated = lax.all_to_all(updated_rows, "obs", split_axis=1, concat_axis=0, tiled=True)
    padded = extended(updated, (("tile", 0),), 1)
    return updated + edge_gain[None, :] * (padded[:-2] + padded[2:] - 2.0 * updated)


def solution(mesh):
    return jax.shard_map(
        local,
        mesh=mesh,
        in_specs=(
            P(("obs", "tile"), None, None),
            P(("obs", "tile"), None),
            P(("obs", "tile")),
            P(("obs", "tile"), None),
            P(("obs", "tile")),
            P("tile", None),
            P(),
            P(),
            P(),
            P(),
            P(),
            P(None, "obs"),
            P("obs"),
        ),
        out_specs=P("tile", "obs"),
        check_vma=False,
    )
```

```python
import functools

import jax
import jax.numpy as jnp
from jax import lax
from jax.experimental import pallas as pl
from jax.experimental.pallas import tpu as pltpu
from jax.sharding import PartitionSpec as P

TILE_DEV = 4
NEG_FLOOR = -1e30
INTERPRET = False


def extended(cells, sides, width):
    for axis, dim in sides:
        count = lax.axis_size(axis)
        head = lax.slice_in_dim(cells, 0, width, axis=dim)
        tail = lax.slice_in_dim(cells, cells.shape[dim] - width, cells.shape[dim], axis=dim)
        cells = jnp.concatenate(
            [
                lax.ppermute(tail, axis, [(i, (i + 1) % count) for i in range(count)]),
                cells,
                lax.ppermute(head, axis, [((i + 1) % count, i) for i in range(count)]),
            ],
            axis=dim,
        )
    return cells


def attend_kernel(kind_ref, tile_ref, raw_ref, bias_ref, w1_ref, w2_ref, kwt_ref, vw_ref, q_ref,
                  m_ref, l_ref, acc_ref, enc_ref, qs_ref, kbd_ref, vbd_ref, p_ref, *, heads, depth):
    slot = pl.program_id(0)

    @pl.when(slot == 0)
    def _():
        m_ref[...] = jnp.full(m_ref.shape, NEG_FLOOR, jnp.float32)
        l_ref[...] = jnp.zeros(l_ref.shape, jnp.float32)
        acc_ref[...] = jnp.zeros(acc_ref.shape, jnp.float32)

    tile = tile_ref[slot]
    kind = kind_ref[slot]
    width = heads * depth
    block_rows = enc_ref.shape[0]
    for k in range(w1_ref.shape[0]):
        @pl.when((tile >= 0) & (kind == k))
        def _():
            pre = jnp.dot(raw_ref[0], w1_ref[k], preferred_element_type=jnp.float32)
            hidden = (pre / (1.0 + jnp.exp(-pre))).astype(jnp.bfloat16)
            enc_ref[...] = jnp.dot(hidden, w2_ref[k], preferred_element_type=jnp.float32).astype(jnp.bfloat16)

    for j in range(q_ref.shape[0]):
        @pl.when(tile == j)
        def _():
            qs_ref[...] = q_ref[j]

    @pl.when(tile >= 0)
    def _():
        encoded = enc_ref[...]
        keys_t = lax.dot_general(
            kwt_ref[...], encoded, (((1,), (1,)), ((), ())), preferred_element_type=jnp.float32
        ).astype(jnp.bfloat16)
        values = jnp.dot(encoded, vw_ref[...], preferred_element_type=jnp.float32).astype(jnp.bfloat16)
        feature_row = lax.broadcasted_iota(jnp.int32, keys_t.shape, 0)
        feature_col = lax.broadcasted_iota(jnp.int32, values.shape, 1)
        for h in range(heads):
            rows = slice(h * block_rows, (h + 1) * block_rows)
            kbd_ref[:, rows] = jnp.where(
                (feature_row >= h * depth) & (feature_row < (h + 1) * depth), keys_t, jnp.zeros_like(keys_t)
            )
            vbd_ref[rows, :] = jnp.where(
                (feature_col >= h * depth) & (feature_col < (h + 1) * depth), values, jnp.zeros_like(values)
            )
        scores = jnp.dot(qs_ref[...], kbd_ref[...], preferred_element_type=jnp.float32)
        bias = bias_ref[0, 0:1, :].astype(jnp.float32)
        scale = depth ** (-0.5)
        peaks, sums = [], []
        for h in range(heads):
            rows = slice(h * block_rows, (h + 1) * block_rows)
            head_scores = scores[:, rows] * scale + bias
            peak = jnp.max(head_scores, axis=1, keepdims=True)
            weights = jnp.exp(head_scores - peak)
            peaks.append(peak)
            sums.append(jnp.sum(weights, axis=1, keepdims=True))
            p_ref[:, rows] = weights.astype(jnp.bfloat16)
        mixture = jnp.dot(p_ref[...], vbd_ref[...], preferred_element_type=jnp.float32)
        for j in range(q_ref.shape[0]):
            @pl.when(tile == j)
            def _():
                for h in range(heads):
                    cols = slice(h * depth, (h + 1) * depth)
                    old_peak = m_ref[j, :, h:h + 1]
                    new_peak = jnp.maximum(old_peak, peaks[h])
                    old_factor = jnp.exp(old_peak - new_peak)
                    new_factor = jnp.exp(peaks[h] - new_peak)
                    m_ref[j, :, h:h + 1] = new_peak
                    l_ref[j, :, h:h + 1] = l_ref[j, :, h:h + 1] * old_factor + sums[h] * new_factor
                    acc_ref[j, :, cols] = acc_ref[j, :, cols] * old_factor + mixture[:, cols] * new_factor


def attend_slots(kinds, tiles, packed, block_rows, first_weight, second_weight, pair_weight, queries, heads):
    slots, _, chans = packed.shape
    tiles_here, latent_rows, width = queries.shape
    depth = width // heads
    key_weight_t = pair_weight[:, :width].T
    value_weight = pair_weight[:, width:]
    const3 = lambda s: (0, 0, 0)
    const2 = lambda s: (0, 0)
    smem = pl.BlockSpec(memory_space=pltpu.SMEM)
    flops = slots * 2 * block_rows * (chans * first_weight.shape[2] + first_weight.shape[2] * width
                                      + width * 2 * width + 2 * latent_rows * width * heads)
    return pl.pallas_call(
        functools.partial(attend_kernel, heads=heads, depth=depth),
        grid=(slots,),
        in_specs=[
            smem,
            smem,
            pl.BlockSpec((1, block_rows, chans), lambda s: (s, 0, 0)),
            pl.BlockSpec((1, 8, chans), lambda s: (s, block_rows // 8, 0)),
            pl.BlockSpec(first_weight.shape, const3),
            pl.BlockSpec(second_weight.shape, const3),
            pl.BlockSpec(key_weight_t.shape, const2),
            pl.BlockSpec(value_weight.shape, const2),
            pl.BlockSpec(queries.shape, const3),
        ],
        out_specs=[
            pl.BlockSpec((tiles_here, latent_rows, heads), const3),
            pl.BlockSpec((tiles_here, latent_rows, heads), const3),
            pl.BlockSpec((tiles_here, latent_rows, width), const3),
        ],
        out_shape=[
            jax.ShapeDtypeStruct((tiles_here, latent_rows, heads), jnp.float32),
            jax.ShapeDtypeStruct((tiles_here, latent_rows, heads), jnp.float32),
            jax.ShapeDtypeStruct((tiles_here, latent_rows, width), jnp.float32),
        ],
        scratch_shapes=[
            pltpu.VMEM((block_rows, width), jnp.bfloat16),
            pltpu.VMEM((latent_rows, width), jnp.bfloat16),
            pltpu.VMEM((width, heads * block_rows), jnp.bfloat16),
            pltpu.VMEM((heads * block_rows, width), jnp.bfloat16),
            pltpu.VMEM((latent_rows, heads * block_rows), jnp.bfloat16),
        ],
        compiler_params=pltpu.CompilerParams(dimension_semantics=("arbitrary",)),
        cost_estimate=pl.CostEstimate(
            flops=int(flops), transcendentals=int(slots * block_rows * (first_weight.shape[2] + heads * latent_rows)),
            bytes_accessed=int(packed.size * 2 + first_weight.size * 2 + second_weight.size * 2
                               + pair_weight.size * 2 + queries.size * 2 + tiles_here * latent_rows * (width + 2 * heads) * 4),
        ),
        interpret=INTERPRET,
    )(kinds, tiles, packed, packed, first_weight, second_weight, key_weight_t, value_weight, queries)


def local(
    raw_obs,
    obs_bias,
    instrument,
    owner,
    local_tile,
    latents,
    first_weight,
    second_weight,
    query_weight,
    pair_weight,
    self_bias,
    out_weight,
    edge_gain,
):
    blocks, block_rows, chans = raw_obs.shape
    owners = lax.axis_size("tile")
    obs_count = lax.axis_size("obs")
    model_width = latents.shape[1]
    head_count = self_bias.shape[0]
    head_depth = model_width // head_count
    tiles_here = TILE_DEV
    slots_each = max(2, 2 * blocks // owners)
    slot_total = owners * slots_each

    targets = owner[:, 0]
    member = (targets[:, None] == jnp.arange(owners, dtype=jnp.int32)[None, :]).astype(jnp.int32)
    slot_rank = jnp.sum(jnp.cumsum(member, axis=0) * member, axis=1) - 1
    position = targets * slots_each + slot_rank
    select = (position[None, :] == jnp.arange(slot_total, dtype=jnp.int32)[:, None]).astype(jnp.bfloat16)
    lane = jnp.arange(chans, dtype=jnp.int32)[None, :]
    tag_row = jnp.where(lane == 0, (local_tile + 1)[:, None], jnp.where(lane == 1, instrument[:, None], 0))
    packed = jnp.concatenate(
        [
            raw_obs,
            obs_bias[:, None, :],
            tag_row[:, None, :].astype(jnp.bfloat16),
            jnp.zeros((blocks, 6, chans), jnp.bfloat16),
        ],
        axis=1,
    )
    placed = jnp.dot(select, packed.reshape(blocks, -1), preferred_element_type=jnp.float32)
    placed = placed.astype(jnp.bfloat16).reshape((slot_total,) + packed.shape[1:])
    received = lax.all_to_all(placed, "tile", split_axis=0, concat_axis=0, tiled=True)
    slot_tags = received[:, block_rows + 1, 0:2].astype(jnp.float32).astype(jnp.int32)
    slot_tiles = slot_tags[:, 0] - 1
    slot_kinds = slot_tags[:, 1]

    queries = jnp.dot(latents, query_weight, preferred_element_type=jnp.float32).astype(jnp.bfloat16)
    part_peak, part_sum, part_mix = attend_slots(
        slot_kinds, slot_tiles, received, block_rows, first_weight, second_weight, pair_weight,
        queries.reshape(tiles_here, -1, model_width), head_count,
    )

    row_total = latents.shape[0]
    share = row_total // obs_count
    partials = jnp.concatenate(
        [
            part_mix.reshape(row_total, model_width),
            part_peak.reshape(row_total, head_count),
            part_sum.reshape(row_total, head_count),
        ],
        axis=1,
    )
    mine = lax.all_to_all(partials, "obs", split_axis=0, concat_axis=0, tiled=True)
    mine = mine.reshape(obs_count, share, model_width + 2 * head_count)
    mix_o = mine[..., :model_width].reshape(obs_count, share, head_count, head_depth)
    peak_o = mine[..., model_width:model_width + head_count]
    sum_o = mine[..., model_width + head_count:]

    row_start = lax.axis_index("obs") * share
    latent_mine = lax.dynamic_slice_in_dim(latents, row_start, share, 0)
    query_mine = lax.dynamic_slice_in_dim(queries, row_start, share, 0).reshape(share, head_count, head_depth)
    self_pair = jnp.dot(latent_mine, pair_weight, preferred_element_type=jnp.float32).astype(jnp.bfloat16)
    self_keys = self_pair[:, :model_width].reshape(share, head_count, head_depth)
    self_values = self_pair[:, model_width:].reshape(share, head_count, head_depth)
    self_score = (
        jnp.sum(query_mine.astype(jnp.float32) * self_keys.astype(jnp.float32), axis=-1)
        * head_depth ** (-0.5)
        + self_bias
    )
    peak = jnp.maximum(jnp.max(peak_o, axis=0), self_score)
    factor_o = jnp.exp(peak_o - peak[None])
    factor_s = jnp.exp(self_score - peak)
    total = factor_s + jnp.sum(factor_o * sum_o, axis=0)
    mixture = factor_s[..., None] * self_values.astype(jnp.float32) + jnp.sum(
        factor_o[..., None] * mix_o, axis=0
    )
    attended = (mixture / total[..., None]).reshape(share, model_width).astype(jnp.bfloat16)
    attended = lax.all_to_all(
        jnp.broadcast_to(attended[None], (obs_count,) + attended.shape), "obs", split_axis=0, concat_axis=0, tiled=True
    ).reshape(obs_count * share, model_width)

    column_count = out_weight.shape[1]
    column_start = lax.axis_index("obs") * column_count
    latent_columns = lax.dynamic_slice_in_dim(latents, column_start, column_count, 1).astype(
        jnp.float32
    )
    updated = latent_columns + jnp.dot(attended, out_weight, preferred_element_type=jnp.float32)
    padded = extended(updated, (("tile", 0),), 1)
    return updated + edge_gain[None, :] * (padded[:-2] + padded[2:] - 2.0 * updated)


def solution(mesh):
    return jax.shard_map(
        local,
        mesh=mesh,
        in_specs=(
            P(("obs", "tile"), None, None),
            P(("obs", "tile"), None),
            P(("obs", "tile")),
            P(("obs", "tile"), None),
            P(("obs", "tile")),
            P("tile", None),
            P(),
            P(),
            P(),
            P(),
            P(),
            P(None, "obs"),
            P("obs"),
        ),
        out_specs=P("tile", "obs"),
        check_vma=False,
    )
```

```python
import functools

import jax
import jax.numpy as jnp
from jax import lax
from jax.experimental import pallas as pl
from jax.experimental.pallas import tpu as pltpu
from jax.sharding import PartitionSpec as P

TILE_DEV = 4
NEG_FLOOR = -1e30
INTERPRET = False


def extended(cells, sides, width):
    for axis, dim in sides:
        count = lax.axis_size(axis)
        head = lax.slice_in_dim(cells, 0, width, axis=dim)
        tail = lax.slice_in_dim(cells, cells.shape[dim] - width, cells.shape[dim], axis=dim)
        cells = jnp.concatenate(
            [
                lax.ppermute(tail, axis, [(i, (i + 1) % count) for i in range(count)]),
                cells,
                lax.ppermute(head, axis, [((i + 1) % count, i) for i in range(count)]),
            ],
            axis=dim,
        )
    return cells


def attend_kernel(kind_ref, tile_ref, raw_ref, bias_ref, w1_ref, w2_ref, kwt_ref, vw_ref, q_ref,
                  m_ref, l_ref, acc_ref, enc_ref, qs_ref, kbd_ref, vbd_ref, p_ref, *, heads, depth):
    slot = pl.program_id(0)

    @pl.when(slot == 0)
    def _():
        m_ref[...] = jnp.full(m_ref.shape, NEG_FLOOR, jnp.float32)
        l_ref[...] = jnp.zeros(l_ref.shape, jnp.float32)
        acc_ref[...] = jnp.zeros(acc_ref.shape, jnp.float32)

    tile = tile_ref[slot]
    kind = kind_ref[slot]
    width = heads * depth
    block_rows = enc_ref.shape[0]
    for k in range(w1_ref.shape[0]):
        @pl.when((tile >= 0) & (kind == k))
        def _():
            pre = jnp.dot(raw_ref[0], w1_ref[k], preferred_element_type=jnp.float32)
            hidden = (pre / (1.0 + jnp.exp(-pre))).astype(jnp.bfloat16)
            enc_ref[...] = jnp.dot(hidden, w2_ref[k], preferred_element_type=jnp.float32).astype(jnp.bfloat16)

    for j in range(q_ref.shape[0]):
        @pl.when(tile == j)
        def _():
            qs_ref[...] = q_ref[j]

    @pl.when(tile >= 0)
    def _():
        encoded = enc_ref[...]
        keys_t = lax.dot_general(
            kwt_ref[...], encoded, (((1,), (1,)), ((), ())), preferred_element_type=jnp.float32
        ).astype(jnp.bfloat16)
        values = jnp.dot(encoded, vw_ref[...], preferred_element_type=jnp.float32).astype(jnp.bfloat16)
        feature_row = lax.broadcasted_iota(jnp.int32, keys_t.shape, 0)
        feature_col = lax.broadcasted_iota(jnp.int32, values.shape, 1)
        for h in range(heads):
            rows = slice(h * block_rows, (h + 1) * block_rows)
            kbd_ref[:, rows] = jnp.where(
                (feature_row >= h * depth) & (feature_row < (h + 1) * depth), keys_t, jnp.zeros_like(keys_t)
            )
            vbd_ref[rows, :] = jnp.where(
                (feature_col >= h * depth) & (feature_col < (h + 1) * depth), values, jnp.zeros_like(values)
            )
        scores = jnp.dot(qs_ref[...], kbd_ref[...], preferred_element_type=jnp.float32)
        bias = bias_ref[0, 0:1, :].astype(jnp.float32)
        scale = depth ** (-0.5)
        peaks, sums = [], []
        for h in range(heads):
            rows = slice(h * block_rows, (h + 1) * block_rows)
            head_scores = scores[:, rows] * scale + bias
            peak = jnp.max(head_scores, axis=1, keepdims=True)
            weights = jnp.exp(head_scores - peak)
            peaks.append(peak)
            sums.append(jnp.sum(weights, axis=1, keepdims=True))
            p_ref[:, rows] = weights.astype(jnp.bfloat16)
        mixture = jnp.dot(p_ref[...], vbd_ref[...], preferred_element_type=jnp.float32)
        for j in range(q_ref.shape[0]):
            @pl.when(tile == j)
            def _():
                for h in range(heads):
                    cols = slice(h * depth, (h + 1) * depth)
                    old_peak = m_ref[j, :, h:h + 1]
                    new_peak = jnp.maximum(old_peak, peaks[h])
                    old_factor = jnp.exp(old_peak - new_peak)
                    new_factor = jnp.exp(peaks[h] - new_peak)
                    m_ref[j, :, h:h + 1] = new_peak
                    l_ref[j, :, h:h + 1] = l_ref[j, :, h:h + 1] * old_factor + sums[h] * new_factor
                    acc_ref[j, :, cols] = acc_ref[j, :, cols] * old_factor + mixture[:, cols] * new_factor


def attend_slots(kinds, tiles, packed, block_rows, first_weight, second_weight, pair_weight, queries, heads):
    slots, _, chans = packed.shape
    tiles_here, latent_rows, width = queries.shape
    depth = width // heads
    key_weight_t = pair_weight[:, :width].T
    value_weight = pair_weight[:, width:]
    const3 = lambda s: (0, 0, 0)
    const2 = lambda s: (0, 0)
    smem = pl.BlockSpec(memory_space=pltpu.SMEM)
    flops = slots * 2 * block_rows * (chans * first_weight.shape[2] + first_weight.shape[2] * width
                                      + width * 2 * width + 2 * latent_rows * width * heads)
    return pl.pallas_call(
        functools.partial(attend_kernel, heads=heads, depth=depth),
        grid=(slots,),
        in_specs=[
            smem,
            smem,
            pl.BlockSpec((1, block_rows, chans), lambda s: (s, 0, 0)),
            pl.BlockSpec((1, 8, chans), lambda s: (s, block_rows // 8, 0)),
            pl.BlockSpec(first_weight.shape, const3),
            pl.BlockSpec(second_weight.shape, const3),
            pl.BlockSpec(key_weight_t.shape, const2),
            pl.BlockSpec(value_weight.shape, const2),
            pl.BlockSpec(queries.shape, const3),
        ],
        out_specs=[
            pl.BlockSpec((tiles_here, latent_rows, heads), const3),
            pl.BlockSpec((tiles_here, latent_rows, heads), const3),
            pl.BlockSpec((tiles_here, latent_rows, width), const3),
        ],
        out_shape=[
            jax.ShapeDtypeStruct((tiles_here, latent_rows, heads), jnp.float32),
            jax.ShapeDtypeStruct((tiles_here, latent_rows, heads), jnp.float32),
            jax.ShapeDtypeStruct((tiles_here, latent_rows, width), jnp.float32),
        ],
        scratch_shapes=[
            pltpu.VMEM((block_rows, width), jnp.bfloat16),
            pltpu.VMEM((latent_rows, width), jnp.bfloat16),
            pltpu.VMEM((width, heads * block_rows), jnp.bfloat16),
            pltpu.VMEM((heads * block_rows, width), jnp.bfloat16),
            pltpu.VMEM((latent_rows, heads * block_rows), jnp.bfloat16),
        ],
        compiler_params=pltpu.CompilerParams(dimension_semantics=("arbitrary",)),
        cost_estimate=pl.CostEstimate(
            flops=int(flops), transcendentals=int(slots * block_rows * (first_weight.shape[2] + heads * latent_rows)),
            bytes_accessed=int(packed.size * 2 + first_weight.size * 2 + second_weight.size * 2
                               + pair_weight.size * 2 + queries.size * 2 + tiles_here * latent_rows * (width + 2 * heads) * 4),
        ),
        interpret=INTERPRET,
    )(kinds, tiles, packed, packed, first_weight, second_weight, key_weight_t, value_weight, queries)


def local(
    raw_obs,
    obs_bias,
    instrument,
    owner,
    local_tile,
    latents,
    first_weight,
    second_weight,
    query_weight,
    pair_weight,
    self_bias,
    out_weight,
    edge_gain,
):
    blocks, block_rows, chans = raw_obs.shape
    owners = lax.axis_size("tile")
    obs_count = lax.axis_size("obs")
    model_width = latents.shape[1]
    head_count = self_bias.shape[0]
    head_depth = model_width // head_count
    tiles_here = TILE_DEV
    slots_each = max(2, 2 * blocks // owners)
    slot_total = owners * slots_each

    targets = owner[:, 0]
    member = (targets[:, None] == jnp.arange(owners, dtype=jnp.int32)[None, :]).astype(jnp.int32)
    slot_rank = jnp.sum(jnp.cumsum(member, axis=0) * member, axis=1) - 1
    position = targets * slots_each + slot_rank
    lane = jnp.arange(chans, dtype=jnp.int32)[None, :]
    tag_row = jnp.where(lane == 0, (local_tile + 1)[:, None], jnp.where(lane == 1, instrument[:, None], 0))
    packed = jnp.concatenate(
        [
            raw_obs,
            obs_bias[:, None, :],
            tag_row[:, None, :].astype(jnp.bfloat16),
            jnp.zeros((blocks, 6, chans), jnp.bfloat16),
        ],
        axis=1,
    )
    source = jnp.full((slot_total,), -1, jnp.int32).at[position].set(
        jnp.arange(blocks, dtype=jnp.int32), mode="drop"
    )
    placed = jnp.where(
        (source >= 0)[:, None, None], jnp.take(packed, jnp.maximum(source, 0), axis=0), jnp.zeros((), packed.dtype)
    )
    received = lax.all_to_all(placed, "tile", split_axis=0, concat_axis=0, tiled=True)
    slot_tags = received[:, block_rows + 1, 0:2].astype(jnp.float32).astype(jnp.int32)
    slot_tiles = slot_tags[:, 0] - 1
    slot_kinds = slot_tags[:, 1]

    queries = jnp.dot(latents, query_weight, preferred_element_type=jnp.float32).astype(jnp.bfloat16)
    part_peak, part_sum, part_mix = attend_slots(
        slot_kinds, slot_tiles, received, block_rows, first_weight, second_weight, pair_weight,
        queries.reshape(tiles_here, -1, model_width), head_count,
    )

    row_total = latents.shape[0]
    share = row_total // obs_count
    partials = jnp.concatenate(
        [
            part_mix.reshape(row_total, model_width),
            part_peak.reshape(row_total, head_count),
            part_sum.reshape(row_total, head_count),
        ],
        axis=1,
    )
    mine = lax.all_to_all(partials, "obs", split_axis=0, concat_axis=0, tiled=True)
    mine = mine.reshape(obs_count, share, model_width + 2 * head_count)
    mix_o = mine[..., :model_width].reshape(obs_count, share, head_count, head_depth)
    peak_o = mine[..., model_width:model_width + head_count]
    sum_o = mine[..., model_width + head_count:]

    row_start = lax.axis_index("obs") * share
    latent_mine = lax.dynamic_slice_in_dim(latents, row_start, share, 0)
    query_mine = lax.dynamic_slice_in_dim(queries, row_start, share, 0).reshape(share, head_count, head_depth)
    self_pair = jnp.dot(latent_mine, pair_weight, preferred_element_type=jnp.float32).astype(jnp.bfloat16)
    self_keys = self_pair[:, :model_width].reshape(share, head_count, head_depth)
    self_values = self_pair[:, model_width:].reshape(share, head_count, head_depth)
    self_score = (
        jnp.sum(query_mine.astype(jnp.float32) * self_keys.astype(jnp.float32), axis=-1)
        * head_depth ** (-0.5)
        + self_bias
    )
    peak = jnp.maximum(jnp.max(peak_o, axis=0), self_score)
    factor_o = jnp.exp(peak_o - peak[None])
    factor_s = jnp.exp(self_score - peak)
    total = factor_s + jnp.sum(factor_o * sum_o, axis=0)
    mixture = factor_s[..., None] * self_values.astype(jnp.float32) + jnp.sum(
        factor_o[..., None] * mix_o, axis=0
    )
    attended = (mixture / total[..., None]).reshape(share, model_width).astype(jnp.bfloat16)
    attended = lax.all_gather(attended, "obs", axis=0, tiled=True)

    column_count = out_weight.shape[1]
    column_start = lax.axis_index("obs") * column_count
    latent_columns = lax.dynamic_slice_in_dim(latents, column_start, column_count, 1).astype(
        jnp.float32
    )
    updated = latent_columns + jnp.dot(attended, out_weight, preferred_element_type=jnp.float32)
    padded = extended(updated, (("tile", 0),), 1)
    return updated + edge_gain[None, :] * (padded[:-2] + padded[2:] - 2.0 * updated)


def solution(mesh):
    return jax.shard_map(
        local,
        mesh=mesh,
        in_specs=(
            P(("obs", "tile"), None, None),
            P(("obs", "tile"), None),
            P(("obs", "tile")),
            P(("obs", "tile"), None),
            P(("obs", "tile")),
            P("tile", None),
            P(),
            P(),
            P(),
            P(),
            P(),
            P(None, "obs"),
            P("obs"),
        ),
        out_specs=P("tile", "obs"),
        check_vma=False,
    )
```

```python
import functools

import jax
import jax.numpy as jnp
from jax import lax
from jax.experimental import pallas as pl
from jax.experimental.pallas import tpu as pltpu
from jax.sharding import PartitionSpec as P

TILE_DEV = 4
NEG_FLOOR = -1e30
INTERPRET = False


def extended(cells, sides, width):
    for axis, dim in sides:
        count = lax.axis_size(axis)
        head = lax.slice_in_dim(cells, 0, width, axis=dim)
        tail = lax.slice_in_dim(cells, cells.shape[dim] - width, cells.shape[dim], axis=dim)
        cells = jnp.concatenate(
            [
                lax.ppermute(tail, axis, [(i, (i + 1) % count) for i in range(count)]),
                cells,
                lax.ppermute(head, axis, [((i + 1) % count, i) for i in range(count)]),
            ],
            axis=dim,
        )
    return cells


def attend_kernel(kind_ref, tile_ref, raw_ref, bias_ref, w1_ref, w2_ref, kwt_ref, vw_ref, q_ref,
                  m_ref, l_ref, acc_ref, enc_ref, qs_ref, kbd_ref, vbd_ref, p_ref, *, heads, depth):
    slot = pl.program_id(0)

    @pl.when(slot == 0)
    def _():
        m_ref[...] = jnp.full(m_ref.shape, NEG_FLOOR, jnp.float32)
        l_ref[...] = jnp.zeros(l_ref.shape, jnp.float32)
        acc_ref[...] = jnp.zeros(acc_ref.shape, jnp.float32)

    tile = tile_ref[slot]
    kind = kind_ref[slot]
    width = heads * depth
    block_rows = enc_ref.shape[0]
    for k in range(w1_ref.shape[0]):
        @pl.when((tile >= 0) & (kind == k))
        def _():
            pre = jnp.dot(raw_ref[0], w1_ref[k], preferred_element_type=jnp.float32)
            hidden = (pre / (1.0 + jnp.exp(-pre))).astype(jnp.bfloat16)
            enc_ref[...] = jnp.dot(hidden, w2_ref[k], preferred_element_type=jnp.float32).astype(jnp.bfloat16)

    for j in range(q_ref.shape[0]):
        @pl.when(tile == j)
        def _():
            qs_ref[...] = q_ref[j]

    @pl.when(tile >= 0)
    def _():
        encoded = enc_ref[...]
        keys_t = lax.dot_general(
            kwt_ref[...], encoded, (((1,), (1,)), ((), ())), preferred_element_type=jnp.float32
        ).astype(jnp.bfloat16)
        values = jnp.dot(encoded, vw_ref[...], preferred_element_type=jnp.float32).astype(jnp.bfloat16)
        feature_row = lax.broadcasted_iota(jnp.int32, keys_t.shape, 0)
        feature_col = lax.broadcasted_iota(jnp.int32, values.shape, 1)
        for h in range(heads):
            rows = slice(h * block_rows, (h + 1) * block_rows)
            kbd_ref[:, rows] = jnp.where(
                (feature_row >= h * depth) & (feature_row < (h + 1) * depth), keys_t, jnp.zeros_like(keys_t)
            )
            vbd_ref[rows, :] = jnp.where(
                (feature_col >= h * depth) & (feature_col < (h + 1) * depth), values, jnp.zeros_like(values)
            )
        scores = jnp.dot(qs_ref[...], kbd_ref[...], preferred_element_type=jnp.float32)
        bias = bias_ref[0, 0:1, :].astype(jnp.float32)
        scale = depth ** (-0.5)
        peaks, sums = [], []
        for h in range(heads):
            rows = slice(h * block_rows, (h + 1) * block_rows)
            head_scores = scores[:, rows] * scale + bias
            peak = jnp.max(head_scores, axis=1, keepdims=True)
            weights = jnp.exp(head_scores - peak)
            peaks.append(peak)
            sums.append(jnp.sum(weights, axis=1, keepdims=True))
            p_ref[:, rows] = weights.astype(jnp.bfloat16)
        mixture = jnp.dot(p_ref[...], vbd_ref[...], preferred_element_type=jnp.float32)
        for j in range(q_ref.shape[0]):
            @pl.when(tile == j)
            def _():
                for h in range(heads):
                    cols = slice(h * depth, (h + 1) * depth)
                    old_peak = m_ref[j, :, h:h + 1]
                    new_peak = jnp.maximum(old_peak, peaks[h])
                    old_factor = jnp.exp(old_peak - new_peak)
                    new_factor = jnp.exp(peaks[h] - new_peak)
                    m_ref[j, :, h:h + 1] = new_peak
                    l_ref[j, :, h:h + 1] = l_ref[j, :, h:h + 1] * old_factor + sums[h] * new_factor
                    acc_ref[j, :, cols] = acc_ref[j, :, cols] * old_factor + mixture[:, cols] * new_factor


def attend_slots(kinds, tiles, packed, block_rows, first_weight, second_weight, pair_weight, queries, heads):
    slots, _, chans = packed.shape
    tiles_here, latent_rows, width = queries.shape
    depth = width // heads
    key_weight_t = pair_weight[:, :width].T
    value_weight = pair_weight[:, width:]
    const3 = lambda s: (0, 0, 0)
    const2 = lambda s: (0, 0)
    smem = pl.BlockSpec(memory_space=pltpu.SMEM)
    flops = slots * 2 * block_rows * (chans * first_weight.shape[2] + first_weight.shape[2] * width
                                      + width * 2 * width + 2 * latent_rows * width * heads)
    return pl.pallas_call(
        functools.partial(attend_kernel, heads=heads, depth=depth),
        grid=(slots,),
        in_specs=[
            smem,
            smem,
            pl.BlockSpec((1, block_rows, chans), lambda s: (s, 0, 0)),
            pl.BlockSpec((1, 8, chans), lambda s: (s, block_rows // 8, 0)),
            pl.BlockSpec(first_weight.shape, const3),
            pl.BlockSpec(second_weight.shape, const3),
            pl.BlockSpec(key_weight_t.shape, const2),
            pl.BlockSpec(value_weight.shape, const2),
            pl.BlockSpec(queries.shape, const3),
        ],
        out_specs=[
            pl.BlockSpec((tiles_here, latent_rows, heads), const3),
            pl.BlockSpec((tiles_here, latent_rows, heads), const3),
            pl.BlockSpec((tiles_here, latent_rows, width), const3),
        ],
        out_shape=[
            jax.ShapeDtypeStruct((tiles_here, latent_rows, heads), jnp.float32),
            jax.ShapeDtypeStruct((tiles_here, latent_rows, heads), jnp.float32),
            jax.ShapeDtypeStruct((tiles_here, latent_rows, width), jnp.float32),
        ],
        scratch_shapes=[
            pltpu.VMEM((block_rows, width), jnp.bfloat16),
            pltpu.VMEM((latent_rows, width), jnp.bfloat16),
            pltpu.VMEM((width, heads * block_rows), jnp.bfloat16),
            pltpu.VMEM((heads * block_rows, width), jnp.bfloat16),
            pltpu.VMEM((latent_rows, heads * block_rows), jnp.bfloat16),
        ],
        compiler_params=pltpu.CompilerParams(dimension_semantics=("arbitrary",)),
        cost_estimate=pl.CostEstimate(
            flops=int(flops), transcendentals=int(slots * block_rows * (first_weight.shape[2] + heads * latent_rows)),
            bytes_accessed=int(packed.size * 2 + first_weight.size * 2 + second_weight.size * 2
                               + pair_weight.size * 2 + queries.size * 2 + tiles_here * latent_rows * (width + 2 * heads) * 4),
        ),
        interpret=INTERPRET,
    )(kinds, tiles, packed, packed, first_weight, second_weight, key_weight_t, value_weight, queries)


def local(
    raw_obs,
    obs_bias,
    instrument,
    owner,
    local_tile,
    latents,
    first_weight,
    second_weight,
    query_weight,
    pair_weight,
    self_bias,
    out_weight,
    edge_gain,
):
    blocks, block_rows, chans = raw_obs.shape
    owners = lax.axis_size("tile")
    obs_count = lax.axis_size("obs")
    model_width = latents.shape[1]
    head_count = self_bias.shape[0]
    head_depth = model_width // head_count
    tiles_here = TILE_DEV
    slots_each = max(2, 2 * blocks // owners)
    slot_total = owners * slots_each

    targets = owner[:, 0]
    member = (targets[:, None] == jnp.arange(owners, dtype=jnp.int32)[None, :]).astype(jnp.int32)
    slot_rank = jnp.sum(jnp.cumsum(member, axis=0) * member, axis=1) - 1
    position = targets * slots_each + slot_rank
    select = (position[None, :] == jnp.arange(slot_total, dtype=jnp.int32)[:, None]).astype(jnp.bfloat16)
    lane = jnp.arange(chans, dtype=jnp.int32)[None, :]
    tag_row = jnp.where(lane == 0, (local_tile + 1)[:, None], jnp.where(lane == 1, instrument[:, None], 0))
    packed = jnp.concatenate(
        [
            raw_obs,
            obs_bias[:, None, :],
            tag_row[:, None, :].astype(jnp.bfloat16),
            jnp.zeros((blocks, 6, chans), jnp.bfloat16),
        ],
        axis=1,
    )
    placed = jnp.dot(select, packed.reshape(blocks, -1), preferred_element_type=jnp.float32)
    placed = placed.astype(jnp.bfloat16).reshape((slot_total,) + packed.shape[1:])
    received = lax.all_to_all(placed, "tile", split_axis=0, concat_axis=0, tiled=True)
    slot_tags = received[:, block_rows + 1, 0:2].astype(jnp.float32).astype(jnp.int32)
    slot_tiles = slot_tags[:, 0] - 1
    slot_kinds = slot_tags[:, 1]

    queries = jnp.dot(latents, query_weight, preferred_element_type=jnp.float32).astype(jnp.bfloat16)
    part_peak, part_sum, part_mix = attend_slots(
        slot_kinds, slot_tiles, received, block_rows, first_weight, second_weight, pair_weight,
        queries.reshape(tiles_here, -1, model_width), head_count,
    )

    row_total = latents.shape[0]
    share = row_total // obs_count
    stats = jnp.concatenate(
        [part_peak.reshape(row_total, head_count), part_sum.reshape(row_total, head_count)], axis=1
    )
    stat_rows = -(-share * 2 * head_count // model_width)
    stats = stats.reshape(obs_count, share * 2 * head_count)
    stats = jnp.pad(stats, ((0, 0), (0, stat_rows * model_width - share * 2 * head_count)))
    partials = jnp.concatenate(
        [
            part_mix.reshape(obs_count, share, model_width),
            stats.reshape(obs_count, stat_rows, model_width),
        ],
        axis=1,
    )
    mine = lax.all_to_all(partials, "obs", split_axis=0, concat_axis=0, tiled=True)
    mix_o = mine[:, :share].reshape(obs_count, share, head_count, head_depth)
    stats_o = mine[:, share:].reshape(obs_count, stat_rows * model_width)[:, :share * 2 * head_count]
    stats_o = stats_o.reshape(obs_count, share, 2 * head_count)
    peak_o = stats_o[..., :head_count]
    sum_o = stats_o[..., head_count:]

    row_start = lax.axis_index("obs") * share
    latent_mine = lax.dynamic_slice_in_dim(latents, row_start, share, 0)
    query_mine = lax.dynamic_slice_in_dim(queries, row_start, share, 0).reshape(share, head_count, head_depth)
    self_pair = jnp.dot(latent_mine, pair_weight, preferred_element_type=jnp.float32).astype(jnp.bfloat16)
    self_keys = self_pair[:, :model_width].reshape(share, head_count, head_depth)
    self_values = self_pair[:, model_width:].reshape(share, head_count, head_depth)
    self_score = (
        jnp.sum(query_mine.astype(jnp.float32) * self_keys.astype(jnp.float32), axis=-1)
        * head_depth ** (-0.5)
        + self_bias
    )
    peak = jnp.maximum(jnp.max(peak_o, axis=0), self_score)
    factor_o = jnp.exp(peak_o - peak[None])
    factor_s = jnp.exp(self_score - peak)
    total = factor_s + jnp.sum(factor_o * sum_o, axis=0)
    mixture = factor_s[..., None] * self_values.astype(jnp.float32) + jnp.sum(
        factor_o[..., None] * mix_o, axis=0
    )
    attended = (mixture / total[..., None]).reshape(share, model_width).astype(jnp.bfloat16)
    attended = lax.all_gather(attended, "obs", axis=0, tiled=True)

    column_count = out_weight.shape[1]
    column_start = lax.axis_index("obs") * column_count
    latent_columns = lax.dynamic_slice_in_dim(latents, column_start, column_count, 1).astype(
        jnp.float32
    )
    updated = latent_columns + jnp.dot(attended, out_weight, preferred_element_type=jnp.float32)
    padded = extended(updated, (("tile", 0),), 1)
    return updated + edge_gain[None, :] * (padded[:-2] + padded[2:] - 2.0 * updated)


def solution(mesh):
    return jax.shard_map(
        local,
        mesh=mesh,
        in_specs=(
            P(("obs", "tile"), None, None),
            P(("obs", "tile"), None),
            P(("obs", "tile")),
            P(("obs", "tile"), None),
            P(("obs", "tile")),
            P("tile", None),
            P(),
            P(),
            P(),
            P(),
            P(),
            P(None, "obs"),
            P("obs"),
        ),
        out_specs=P("tile", "obs"),
        check_vma=False,
    )
```
